32 devices in a mesh: lines: 2 (over x), col: 16 (over z, y, core).
Axes of the slice: x: 2, y: 2, z: 4, core: 2. Of those that a mesh axis runs over, the one named last changes fastest.
Arguments:
- primary: float32 [16, 4, 128, 256], P(None, 'lines', 'col'), parts along dimension 1, may hold values from -6 to 6
- conductivity: float32 [128, 512], P('col', 'lines'), parts along dimension 1, may hold values from 0.1 to 10
- wavenumbers: float32 [16], replicated, may hold values from 0.05 to 1.5
- quadrature: float32 [16], replicated, may hold values from 0.02 to 0.2
- electrodes: int32 [64], P(('lines', 'col')), parts along dimension 0, may hold values from 0 to 127, as said below
- far_pole: int32 [4, 32], P('lines'), parts along dimension 0, may hold values from 0 to 31, as said below
- observed: float32 [4, 32], P('lines'), parts along dimension 0, may hold values from -6 to 6
- prior_adjoint: float32 [16, 4, 128, 256], P(None, 'lines', 'col'), parts along dimension 1, may hold values from -0.012 to 0.012
Outputs:
- predicted: float32 [4, 32], P('lines'), parts along dimension 0
- gradient: float32 [128, 512], P('col', 'lines'), parts along dimension 1
The draws below stay inside these ranges and needn't reach their ends.
There are 2 independent parts, one for each index of `lines`. The reference program is written for one: setup_inputs(seed, part) draws one part's arguments, and reference() takes and returns one part's arrays. A program takes and returns all parts, laid end to end along the dimension named above; an argument that names none is the same for every part. Nothing has to cross between parts.
Inputs may be any that keep to these rules, and one draw needn't show every extreme that they name: electrodes[e] lies in columns 4 e to 4 e + 3. far_pole[s, r] differs from r by 1 to 8.
All inputs are finite; a program needn't handle non-finite values.
Results may differ from the reference program's by a relative error of at most 0.0003.
Values sent between devices are 32-bit elements; how exact they have to be, the bound alone decides.
No kernel may reach another device: no remote copies, remote signals or barrier semaphores. Data moves between devices by JAX's collectives and lax.ppermute only.
A program may use at most 64 MiB of HBM per device.

```python
import math
import jax
import jax.numpy as jnp
from jax import lax

WAVES = 16
SOURCES = 2
NZ = 256
ITERS = 2
SPREAD = 8
ELECTRODES = 32
NX = 128


def draw_electrodes(key, part):
    numbers = jnp.arange(ELECTRODES)
    shifted = jax.random.randint(key, (ELECTRODES,), 0, 4)
    shifted = jnp.where(numbers == 0, 0, jnp.where(numbers == ELECTRODES - 1, 3, shifted))
    return (4 * numbers + shifted).astype(jnp.int32)


def draw_far_pole(key, part):
    numbers = jnp.arange(ELECTRODES)[None, :]
    spacing = jax.random.randint(jax.random.fold_in(key, 1), (SOURCES, ELECTRODES), 1, SPREAD + 1)
    coin = jax.random.randint(jax.random.fold_in(key, 2), (SOURCES, ELECTRODES), 0, 2)
    forced = (numbers == 1) | (numbers == ELECTRODES - 2)
    spacing = jnp.where(forced, 1, spacing)
    ahead = numbers + spacing
    behind = numbers - spacing
    use_behind = (behind >= 0) & ((coin == 1) | (ahead >= ELECTRODES))
    use_behind = jnp.where(numbers == 1, True, jnp.where(numbers == ELECTRODES - 2, False, use_behind))
    return jnp.where(use_behind, behind, ahead).astype(jnp.int32)


def block_scale(key, shape, shards, least, high):
    factor_of = 1.0
    for dim, parts in shards:
        steps = jax.random.uniform(jax.random.fold_in(jax.random.fold_in(key, 6), dim), (parts,), jnp.float32, least / len(shards), high / len(shards))
        factor_of = factor_of * jnp.repeat(jnp.exp(steps), shape[dim] // parts).reshape((-1,) + (1,) * (len(shape) - 1 - dim))
    return factor_of


def scatter_about(rng, extent, width, most, split=(), kind=jnp.bfloat16):
    gain = block_scale(rng, extent, split, -0.22, 0.18) if split else 1.0
    values = jax.random.normal(rng, extent, jnp.float32) * width * gain
    return jnp.minimum(jnp.maximum(values, -most), most).astype(kind)


def setup_inputs(seed: int = 0, part: int = 0) -> dict:
    keys = jax.random.split(jax.random.key(seed), 9)
    part_keys = jax.random.split(jax.random.fold_in(keys[8], part), 9)
    return {
        "primary": scatter_about(part_keys[0], (WAVES, SOURCES, NX, NZ), 1.0, 6.0, ((2, 16),), jnp.float32),
        "conductivity": jnp.clip(jnp.exp(math.log(10.0) - 4.6051702 * jax.random.uniform(part_keys[1], (NX, NZ), jnp.float32) ** block_scale(part_keys[1], (NX, NZ), ((0, 16),), -0.2, 0.2)), 0.1, 10.0),
        "wavenumbers": jnp.clip(jnp.exp(jax.random.uniform(keys[2], (WAVES,), jnp.float32, math.log(0.05), math.log(1.5))), 0.05, 1.5),
        "quadrature": jnp.clip(jnp.exp(jax.random.uniform(keys[3], (WAVES,), jnp.float32, math.log(0.02), math.log(0.2))), 0.02, 0.2),
        "electrodes": draw_electrodes(jax.random.fold_in(jax.random.fold_in(keys[8], part), 71), part),
        "far_pole": draw_far_pole(jax.random.fold_in(jax.random.fold_in(keys[8], part), 71), part),
        "observed": scatter_about(part_keys[6], (SOURCES, ELECTRODES), 1.0, 6.0, (), jnp.float32),
        "prior_adjoint": scatter_about(part_keys[7], (WAVES, SOURCES, NX, NZ), 0.002, 0.012, ((2, 16),), jnp.float32),
    }


def coefficients(sigma_wide):
    center = sigma_wide[1:-1]
    west_face = 0.5 * (center + sigma_wide[:-2])
    east_face = 0.5 * (center + sigma_wide[2:])
    below_sigma = jnp.concatenate([center[:, 1:], jnp.zeros_like(center[:, :1])], axis=1)
    lower_face = 0.5 * (center + below_sigma)
    above_sigma = jnp.concatenate([jnp.zeros_like(center[:, :1]), center[:, :-1]], axis=1)
    upper_face = 0.5 * (center + above_sigma)
    top_row = jnp.arange(center.shape[1]) == 0
    upper_face = jnp.where(top_row[None, :], 0.0, upper_face)
    return (west_face, east_face, lower_face, upper_face, center)


def stencil(field_wide, faces_set, mass_scale):
    west_face, east_face, lower_face, upper_face, center = faces_set
    middle = field_wide[..., 1:-1, :]
    below_cells = jnp.concatenate([middle[..., 1:], jnp.zeros_like(middle[..., :1])], axis=-1)
    above_cells = jnp.concatenate([jnp.zeros_like(middle[..., :1]), middle[..., :-1]], axis=-1)
    result = west_face * (middle - field_wide[..., :-2, :]) + east_face * (middle - field_wide[..., 2:, :])
    result = result + lower_face * (middle - below_cells) + upper_face * (middle - above_cells)
    return result + mass_scale * center * middle


def conjugate(source, apply_op, start):
    if start is None:
        solution = jnp.zeros_like(source)
        residual = source
    else:
        solution = start
        residual = source - apply_op(start)
    direction = residual
    norm_now = jnp.sum(residual * residual, axis=(1, 2))
    for iteration in range(ITERS):
        applied = apply_op(direction)
        step_size = norm_now / jnp.sum(direction * applied, axis=(1, 2))
        solution = solution + step_size[:, None, None] * direction
        residual = residual - step_size[:, None, None] * applied
        norm_next = jnp.sum(residual * residual, axis=(1, 2))
        direction = residual + (norm_next / norm_now)[:, None, None] * direction
        norm_now = norm_next
    return solution


def reference(primary, conductivity, wavenumbers, quadrature, electrodes, far_pole, observed, prior_adjoint):
    zero_col = jnp.zeros((1, NZ), jnp.float32)
    operator_faces = coefficients(jnp.concatenate([zero_col, conductivity, zero_col], axis=0))
    contrast_faces = coefficients(jnp.concatenate([zero_col, conductivity - 1.0, zero_col], axis=0))

    def pad_field(state):
        edge_zero = jnp.zeros((state.shape[0], 1, NZ), jnp.float32)
        return jnp.concatenate([edge_zero, state, edge_zero], axis=1)

    def forward(primary_k, mass_scale):
        source = -stencil(pad_field(primary_k), contrast_faces, mass_scale)
        secondary = conjugate(source, lambda state: stencil(pad_field(state), operator_faces, mass_scale), None)
        return primary_k + secondary

    def surface_of(inputs_k):
        return forward(inputs_k[0], inputs_k[1] * inputs_k[1])[:, :, 0]

    surfaces = lax.map(surface_of, (primary, wavenumbers))
    weighted = jnp.einsum("k,ksx->sx", quadrature, surfaces, precision=lax.Precision.HIGHEST)
    potentials = jnp.take(weighted, electrodes, axis=1)
    predicted = potentials - jnp.take_along_axis(potentials, far_pole, axis=1)
    misfit = predicted - observed
    source_rows = jnp.arange(SOURCES)[:, None] * jnp.ones_like(far_pole)
    returned = jnp.zeros_like(misfit).at[source_rows, far_pole].add(misfit)
    charge = misfit - returned
    charge_cols = jnp.zeros((SOURCES, NX), jnp.float32).at[:, electrodes].set(charge)
    surface_row = (jnp.arange(NZ) == 0).astype(jnp.float32)

    def accumulate(grad_sum, inputs_k):
        primary_k, wave_k, weight_k, prior_k = inputs_k
        mass_scale = wave_k * wave_k
        total_field = forward(primary_k, mass_scale)
        adjoint_source = weight_k * charge_cols[:, :, None] * surface_row
        adjoint = conjugate(adjoint_source, lambda state: stencil(pad_field(state), operator_faces, mass_scale), prior_k)
        zero_edge = jnp.zeros((SOURCES, 1, NZ), jnp.float32)
        adjoint_next = jnp.concatenate([adjoint[:, 1:], zero_edge], axis=1)
        total_next = jnp.concatenate([total_field[:, 1:], zero_edge], axis=1)
        adjoint_down = jnp.concatenate([adjoint[..., 1:], jnp.zeros_like(adjoint[..., :1])], axis=-1)
        total_down = jnp.concatenate([total_field[..., 1:], jnp.zeros_like(total_field[..., :1])], axis=-1)
        correlation = (adjoint_next - adjoint) * (total_next - total_field)
        correlation = correlation + (adjoint_down - adjoint) * (total_down - total_field)
        correlation = correlation + mass_scale * adjoint * total_field
        return grad_sum + jnp.sum(correlation, axis=0), None

    gradient, unused = lax.scan(accumulate, jnp.zeros((NX, NZ), jnp.float32), (primary, wavenumbers, quadrature, prior_adjoint))
    return (predicted, gradient)
```

```python
import math

import jax
import jax.numpy as jnp
from jax import lax
from jax.sharding import Mesh
from jax.sharding import PartitionSpec as P

ITERS = 2


def halo(block, axis, dim, width):
    count = lax.axis_size(axis)
    edge_shape = list(block.shape)
    edge_shape[dim] = width
    if count == 1:
        zeros = jnp.zeros(edge_shape, block.dtype)
        return jnp.concatenate([zeros, block, zeros], axis=dim)
    forward = [(i, i + 1) for i in range(count - 1)]
    backward = [(target, source) for source, target in forward]
    low = lax.ppermute(
        lax.slice_in_dim(block, block.shape[dim] - width, None, axis=dim), axis, forward
    )
    high = lax.ppermute(lax.slice_in_dim(block, 0, width, axis=dim), axis, backward)
    return jnp.concatenate([low, block, high], axis=dim)


def next_column(field, axis):
    count = lax.axis_size(axis)
    if count == 1:
        edge = jnp.zeros_like(field[:, :, :1])
    else:
        edge = lax.ppermute(field[:, :, :1], axis, [(i + 1, i) for i in range(count - 1)])
    return jnp.concatenate([field[:, :, 1:], edge], axis=2)


def coefficients(sigma_wide):
    center = sigma_wide[1:-1]
    west_face = 0.5 * (center + sigma_wide[:-2])
    east_face = 0.5 * (center + sigma_wide[2:])
    below_sigma = jnp.concatenate([center[:, 1:], jnp.zeros_like(center[:, :1])], axis=1)
    lower_face = 0.5 * (center + below_sigma)
    above_sigma = jnp.concatenate([jnp.zeros_like(center[:, :1]), center[:, :-1]], axis=1)
    upper_face = 0.5 * (center + above_sigma)
    top_row = jnp.arange(center.shape[1]) == 0
    upper_face = jnp.where(top_row[None, :], 0.0, upper_face)
    return (west_face, east_face, lower_face, upper_face, center)


def stencil(field_wide, faces_set, mass_scale):
    west_face, east_face, lower_face, upper_face, center = faces_set
    middle = field_wide[..., 1:-1, :]
    below_cells = jnp.concatenate([middle[..., 1:], jnp.zeros_like(middle[..., :1])], axis=-1)
    above_cells = jnp.concatenate([jnp.zeros_like(middle[..., :1]), middle[..., :-1]], axis=-1)
    result = west_face * (middle - field_wide[..., :-2, :]) + east_face * (
        middle - field_wide[..., 2:, :]
    )
    result = result + lower_face * (middle - below_cells) + upper_face * (middle - above_cells)
    return result + mass_scale * center * middle


def on_device(
    primary, conductivity, wavenumbers, quadrature, electrodes, far_pole, observed, prior_adjoint
):
    groups = lax.axis_size("kq")
    spread = lax.axis_size("cs")
    waves, sources, own_columns, depth = primary.shape
    per_group = waves // groups
    group = lax.axis_index("kq")
    block = lax.axis_index("cs")
    fields = per_group * sources

    def by_group(array):
        return array.reshape(groups, fields, own_columns, depth)

    sigma_copies = jnp.broadcast_to(conductivity[None, None], (groups, 1, own_columns, depth))
    send = jnp.concatenate([by_group(primary), by_group(prior_adjoint), sigma_copies], axis=1)
    if groups > 1:
        send = lax.all_to_all(send, "kq", 0, 2, tiled=True)
    received = send[0]
    width = groups * own_columns
    primary = received[:fields].reshape(per_group, sources, width, depth)
    prior_adjoint = received[fields : 2 * fields].reshape(per_group, sources, width, depth)
    sigma = received[2 * fields]

    columns = width * spread
    offset = block * width
    wide_sigma = halo(sigma, "cs", 0, 2)
    positions = offset - 2 + jnp.arange(width + 4)
    inside = (positions >= 0) & (positions < columns)
    contrast_wide = jnp.where(inside[:, None], wide_sigma - 1.0, 0.0)
    own_waves = lax.dynamic_slice_in_dim(wavenumbers, group * per_group, per_group)
    weights = lax.dynamic_slice_in_dim(quadrature, group * per_group, per_group)
    mass_scale = (own_waves * own_waves)[:, None, None, None]
    operator_faces = coefficients(wide_sigma[1:-1])

    def operate(state):
        return stencil(halo(state, "cs", 2, 1), operator_faces, mass_scale)

    def dots(left, right):
        total = jnp.sum(left * right, axis=(2, 3))
        if spread > 1:
            total = lax.psum(total, "cs")
        return total[:, :, None, None]

    def conjugate(source, start):
        if start is None:
            solution = jnp.zeros_like(source)
            residual = source
        else:
            solution = start
            residual = source - operate(start)
        direction = residual
        norm_now = dots(residual, residual)
        for iteration in range(ITERS):
            applied = operate(direction)
            step_size = norm_now / dots(direction, applied)
            solution = solution + step_size * direction
            if iteration + 1 < ITERS:
                residual = residual - step_size * applied
                norm_next = dots(residual, residual)
                direction = residual + (norm_next / norm_now) * direction
                norm_now = norm_next
        return solution

    source = -stencil(halo(primary, "cs", 2, 1), coefficients(contrast_wide[1:-1]), mass_scale)
    total_field = primary + conjugate(source, None)

    surface = total_field[:, :, :, 0]
    weighted = jnp.sum(weights[:, None, None] * surface, axis=0)
    packet = jnp.concatenate([weighted.reshape(-1), electrodes.astype(jnp.float32)])
    gathered = lax.all_gather(packet, ("cs", "kq"))
    partial = gathered[:, : sources * width].reshape(spread, groups, sources, width)
    line_surface = jnp.sum(partial, axis=1).transpose(1, 0, 2).reshape(sources, columns)
    all_electrodes = gathered[:, sources * width :].reshape(-1).astype(jnp.int32)
    count = all_electrodes.shape[0]

    picks = (all_electrodes[:, None] == jnp.arange(columns)[None, :]).astype(jnp.float32)
    potentials = jnp.sum(line_surface[:, None, :] * picks[None], axis=2)
    pole_hits = (far_pole[:, :, None] == jnp.arange(count)[None, None, :]).astype(jnp.float32)
    far_potentials = jnp.sum(potentials[:, None, :] * pole_hits, axis=2)
    predicted = potentials - far_potentials
    misfit = predicted - observed
    returned = jnp.sum(misfit[:, :, None] * pole_hits, axis=1)
    charge = misfit - returned
    own_picks = (
        all_electrodes[:, None] == offset + jnp.arange(width)[None, :]
    ).astype(jnp.float32)
    charge_cols = jnp.sum(charge[:, :, None] * own_picks[None], axis=1)
    surface_row = (jnp.arange(depth) == 0).astype(jnp.float32)
    adjoint_source = weights[:, None, None, None] * charge_cols[None, :, :, None] * surface_row
    adjoint = conjugate(adjoint_source, prior_adjoint)

    adjoint_next = next_column(adjoint, "cs")
    total_next = next_column(total_field, "cs")
    adjoint_down = jnp.concatenate([adjoint[..., 1:], jnp.zeros_like(adjoint[..., :1])], axis=-1)
    total_down = jnp.concatenate(
        [total_field[..., 1:], jnp.zeros_like(total_field[..., :1])], axis=-1
    )
    correlation = (adjoint_next - adjoint) * (total_next - total_field)
    correlation = correlation + (adjoint_down - adjoint) * (total_down - total_field)
    correlation = correlation + mass_scale * adjoint * total_field
    gradient = jnp.sum(correlation, axis=(0, 1))
    if groups > 1:
        gradient = lax.psum_scatter(gradient, "kq", scatter_dimension=0, tiled=True)
    return (predicted, gradient)


def solution(mesh):
    lines = mesh.shape["lines"]
    col = mesh.shape["col"]

    def run(*arrays):
        groups = math.gcd(col, arrays[0].shape[0])
        split = Mesh(mesh.devices.reshape(lines, col // groups, groups), ("lines", "cs", "kq"))
        cells = ("cs", "kq")
        placed = (
            P(None, "lines", cells, None),
            P(cells, "lines"),
            P(),
            P(),
            P(("lines",) + cells),
            P("lines", None),
            P("lines", None),
            P(None, "lines", cells, None),
        )
        return jax.shard_map(
            on_device,
            mesh=split,
            in_specs=placed,
            out_specs=(P("lines", None), P(cells, "lines")),
            check_vma=False,
        )(*arrays)

    return run
```

```python
import math

import jax
import jax.numpy as jnp
from jax import lax
from jax.sharding import Mesh
from jax.sharding import PartitionSpec as P

ITERS = 2


def halo(block, axis, dim, width):
    count = lax.axis_size(axis)
    edge_shape = list(block.shape)
    edge_shape[dim] = width
    if count == 1:
        zeros = jnp.zeros(edge_shape, block.dtype)
        return jnp.concatenate([zeros, block, zeros], axis=dim)
    forward = [(i, i + 1) for i in range(count - 1)]
    backward = [(target, source) for source, target in forward]
    low = lax.ppermute(
        lax.slice_in_dim(block, block.shape[dim] - width, None, axis=dim), axis, forward
    )
    high = lax.ppermute(lax.slice_in_dim(block, 0, width, axis=dim), axis, backward)
    return jnp.concatenate([low, block, high], axis=dim)


def next_column(field, axis):
    count = lax.axis_size(axis)
    if count == 1:
        edge = jnp.zeros_like(field[:, :, :1])
    else:
        edge = lax.ppermute(field[:, :, :1], axis, [(i + 1, i) for i in range(count - 1)])
    return jnp.concatenate([field[:, :, 1:], edge], axis=2)


def coefficients(sigma_wide):
    center = sigma_wide[1:-1]
    west_face = 0.5 * (center + sigma_wide[:-2])
    east_face = 0.5 * (center + sigma_wide[2:])
    below_sigma = jnp.concatenate([center[:, 1:], jnp.zeros_like(center[:, :1])], axis=1)
    lower_face = 0.5 * (center + below_sigma)
    above_sigma = jnp.concatenate([jnp.zeros_like(center[:, :1]), center[:, :-1]], axis=1)
    upper_face = 0.5 * (center + above_sigma)
    top_row = jnp.arange(center.shape[1]) == 0
    upper_face = jnp.where(top_row[None, :], 0.0, upper_face)
    return (west_face, east_face, lower_face, upper_face, center)


def stencil(field_wide, faces_set, mass_scale):
    west_face, east_face, lower_face, upper_face, center = faces_set
    middle = field_wide[..., 1:-1, :]
    below_cells = jnp.concatenate([middle[..., 1:], jnp.zeros_like(middle[..., :1])], axis=-1)
    above_cells = jnp.concatenate([jnp.zeros_like(middle[..., :1]), middle[..., :-1]], axis=-1)
    result = west_face * (middle - field_wide[..., :-2, :]) + east_face * (
        middle - field_wide[..., 2:, :]
    )
    result = result + lower_face * (middle - below_cells) + upper_face * (middle - above_cells)
    return result + mass_scale * center * middle


def on_device(
    primary, conductivity, wavenumbers, quadrature, electrodes, far_pole, observed, prior_adjoint
):
    groups = lax.axis_size("kq")
    spread = lax.axis_size("cs")
    waves, sources, own_columns, depth = primary.shape
    per_group = waves // groups
    group = lax.axis_index("kq")
    block = lax.axis_index("cs")
    fields = per_group * sources

    def by_group(array):
        return array.reshape(groups, fields, own_columns, depth)

    sigma_copies = jnp.broadcast_to(conductivity[None, None], (groups, 1, own_columns, depth))
    send = jnp.concatenate([by_group(primary), by_group(prior_adjoint), sigma_copies], axis=1)
    if groups > 1:
        send = lax.all_to_all(send, "kq", 0, 2, tiled=True)
    received = send[0]
    width = groups * own_columns
    primary = received[:fields].reshape(per_group, sources, width, depth)
    prior_adjoint = received[fields : 2 * fields].reshape(per_group, sources, width, depth)
    sigma = received[2 * fields]

    columns = width * spread
    offset = block * width
    wide_sigma = halo(sigma, "cs", 0, 2)
    positions = offset - 2 + jnp.arange(width + 4)
    inside = (positions >= 0) & (positions < columns)
    contrast_wide = jnp.where(inside[:, None], wide_sigma - 1.0, 0.0)
    own_waves = lax.dynamic_slice_in_dim(wavenumbers, group * per_group, per_group)
    weights = lax.dynamic_slice_in_dim(quadrature, group * per_group, per_group)
    mass_scale = (own_waves * own_waves)[:, None, None, None]
    operator_faces = coefficients(wide_sigma[1:-1])

    def operate(state):
        return stencil(halo(state, "cs", 2, 1), operator_faces, mass_scale)

    def dots(left, right):
        total = jnp.sum(left * right, axis=(2, 3))
        if spread > 1:
            total = lax.psum(total, "cs")
        return total[:, :, None, None]

    def conjugate(source, start):
        if start is None:
            solution = jnp.zeros_like(source)
            residual = source
        else:
            solution = start
            residual = source - operate(start)
        direction = residual
        norm_now = dots(residual, residual)
        for iteration in range(ITERS):
            applied = operate(direction)
            step_size = norm_now / dots(direction, applied)
            solution = solution + step_size * direction
            if iteration + 1 < ITERS:
                residual = residual - step_size * applied
                norm_next = dots(residual, residual)
                direction = residual + (norm_next / norm_now) * direction
                norm_now = norm_next
        return solution

    source = -stencil(halo(primary, "cs", 2, 1), coefficients(contrast_wide[1:-1]), mass_scale)
    total_field = primary + conjugate(source, None)

    surface = total_field[:, :, :, 0]
    weighted = jnp.sum(weights[:, None, None] * surface, axis=0)
    packet = jnp.concatenate([weighted.reshape(-1), electrodes.astype(jnp.float32)])
    gathered = jnp.broadcast_to(packet[None], (groups,) + packet.shape)
    if groups > 1:
        gathered = lax.all_to_all(gathered, "kq", 0, 0, tiled=True)
    if spread > 1:
        gathered = lax.all_gather(gathered, "cs")
    gathered = gathered.reshape(spread * groups, -1)
    partial = gathered[:, : sources * width].reshape(spread, groups, sources, width)
    line_surface = jnp.sum(partial, axis=1).transpose(1, 0, 2).reshape(sources, columns)
    all_electrodes = gathered[:, sources * width :].reshape(-1).astype(jnp.int32)
    count = all_electrodes.shape[0]

    picks = (all_electrodes[:, None] == jnp.arange(columns)[None, :]).astype(jnp.float32)
    potentials = jnp.sum(line_surface[:, None, :] * picks[None], axis=2)
    pole_hits = (far_pole[:, :, None] == jnp.arange(count)[None, None, :]).astype(jnp.float32)
    far_potentials = jnp.sum(potentials[:, None, :] * pole_hits, axis=2)
    predicted = potentials - far_potentials
    misfit = predicted - observed
    returned = jnp.sum(misfit[:, :, None] * pole_hits, axis=1)
    charge = misfit - returned
    own_picks = (
        all_electrodes[:, None] == offset + jnp.arange(width)[None, :]
    ).astype(jnp.float32)
    charge_cols = jnp.sum(charge[:, :, None] * own_picks[None], axis=1)
    surface_row = (jnp.arange(depth) == 0).astype(jnp.float32)
    adjoint_source = weights[:, None, None, None] * charge_cols[None, :, :, None] * surface_row
    adjoint = conjugate(adjoint_source, prior_adjoint)

    adjoint_next = next_column(adjoint, "cs")
    total_next = next_column(total_field, "cs")
    adjoint_down = jnp.concatenate([adjoint[..., 1:], jnp.zeros_like(adjoint[..., :1])], axis=-1)
    total_down = jnp.concatenate(
        [total_field[..., 1:], jnp.zeros_like(total_field[..., :1])], axis=-1
    )
    correlation = (adjoint_next - adjoint) * (total_next - total_field)
    correlation = correlation + (adjoint_down - adjoint) * (total_down - total_field)
    correlation = correlation + mass_scale * adjoint * total_field
    gradient = jnp.sum(correlation, axis=(0, 1))
    if groups > 1:
        gradient = gradient.reshape(groups, own_columns, depth)
        gradient = jnp.sum(lax.all_to_all(gradient, "kq", 0, 0, tiled=True), axis=0)
    return (predicted, gradient)


def solution(mesh):
    lines = mesh.shape["lines"]
    col = mesh.shape["col"]

    def run(*arrays):
        groups = math.gcd(col, arrays[0].shape[0])
        split = Mesh(mesh.devices.reshape(lines, col // groups, groups), ("lines", "cs", "kq"))
        cells = ("cs", "kq")
        placed = (
            P(None, "lines", cells, None),
            P(cells, "lines"),
            P(),
            P(),
            P(("lines",) + cells),
            P("lines", None),
            P("lines", None),
            P(None, "lines", cells, None),
        )
        return jax.shard_map(
            on_device,
            mesh=split,
            in_specs=placed,
            out_specs=(P("lines", None), P(cells, "lines")),
            check_vma=False,
        )(*arrays)

    return run
```

```python
import math

import jax
import jax.numpy as jnp
from jax import lax
from jax.sharding import Mesh
from jax.sharding import PartitionSpec as P

ITERS = 2


def halo(block, axis, dim, width):
    count = lax.axis_size(axis)
    edge_shape = list(block.shape)
    edge_shape[dim] = width
    if count == 1:
        zeros = jnp.zeros(edge_shape, block.dtype)
        return jnp.concatenate([zeros, block, zeros], axis=dim)
    forward = [(i, i + 1) for i in range(count - 1)]
    backward = [(target, source) for source, target in forward]
    low = lax.ppermute(
        lax.slice_in_dim(block, block.shape[dim] - width, None, axis=dim), axis, forward
    )
    high = lax.ppermute(lax.slice_in_dim(block, 0, width, axis=dim), axis, backward)
    return jnp.concatenate([low, block, high], axis=dim)


def next_column(field, axis):
    count = lax.axis_size(axis)
    if count == 1:
        edge = jnp.zeros_like(field[:, :, :1])
    else:
        edge = lax.ppermute(field[:, :, :1], axis, [(i + 1, i) for i in range(count - 1)])
    return jnp.concatenate([field[:, :, 1:], edge], axis=2)


def coefficients(sigma_wide):
    center = sigma_wide[1:-1]
    west_face = 0.5 * (center + sigma_wide[:-2])
    east_face = 0.5 * (center + sigma_wide[2:])
    below_sigma = jnp.concatenate([center[:, 1:], jnp.zeros_like(center[:, :1])], axis=1)
    lower_face = 0.5 * (center + below_sigma)
    above_sigma = jnp.concatenate([jnp.zeros_like(center[:, :1]), center[:, :-1]], axis=1)
    upper_face = 0.5 * (center + above_sigma)
    top_row = jnp.arange(center.shape[1]) == 0
    upper_face = jnp.where(top_row[None, :], 0.0, upper_face)
    return (west_face, east_face, lower_face, upper_face, center)


def stencil(field_wide, faces_set, mass_scale):
    west_face, east_face, lower_face, upper_face, center = faces_set
    middle = field_wide[..., 1:-1, :]
    below_cells = jnp.concatenate([middle[..., 1:], jnp.zeros_like(middle[..., :1])], axis=-1)
    above_cells = jnp.concatenate([jnp.zeros_like(middle[..., :1]), middle[..., :-1]], axis=-1)
    result = west_face * (middle - field_wide[..., :-2, :]) + east_face * (
        middle - field_wide[..., 2:, :]
    )
    result = result + lower_face * (middle - below_cells) + upper_face * (middle - above_cells)
    return result + mass_scale * center * middle


def on_device(
    primary, conductivity, wavenumbers, quadrature, electrodes, far_pole, observed, prior_adjoint
):
    groups = lax.axis_size("kq")
    spread = lax.axis_size("cs")
    waves, sources, own_columns, depth = primary.shape
    per_group = waves // groups
    group = lax.axis_index("kq")
    block = lax.axis_index("cs")

    width = groups * own_columns
    sigma = jnp.broadcast_to(conductivity[None], (groups, own_columns, depth))
    if groups > 1:
        primary = lax.all_to_all(primary, "kq", 0, 2, tiled=True)
        sigma = lax.all_to_all(sigma, "kq", 0, 1, tiled=True)
        prior_adjoint = lax.all_to_all(prior_adjoint, "kq", 0, 2, tiled=True)
    sigma = sigma[0]

    columns = width * spread
    offset = block * width
    wide_sigma = halo(sigma, "cs", 0, 2)
    positions = offset - 2 + jnp.arange(width + 4)
    inside = (positions >= 0) & (positions < columns)
    contrast_wide = jnp.where(inside[:, None], wide_sigma - 1.0, 0.0)
    own_waves = lax.dynamic_slice_in_dim(wavenumbers, group * per_group, per_group)
    weights = lax.dynamic_slice_in_dim(quadrature, group * per_group, per_group)
    mass_scale = (own_waves * own_waves)[:, None, None, None]
    operator_faces = coefficients(wide_sigma[1:-1])

    def operate(state):
        return stencil(halo(state, "cs", 2, 1), operator_faces, mass_scale)

    def dots(left, right):
        total = jnp.sum(left * right, axis=(2, 3))
        if spread > 1:
            total = lax.psum(total, "cs")
        return total[:, :, None, None]

    def conjugate(source, start):
        if start is None:
            solution = jnp.zeros_like(source)
            residual = source
        else:
            solution = start
            residual = source - operate(start)
        direction = residual
        norm_now = dots(residual, residual)
        for iteration in range(ITERS):
            applied = operate(direction)
            step_size = norm_now / dots(direction, applied)
            solution = solution + step_size * direction
            if iteration + 1 < ITERS:
                residual = residual - step_size * applied
                norm_next = dots(residual, residual)
                direction = residual + (norm_next / norm_now) * direction
                norm_now = norm_next
        return solution

    source = -stencil(halo(primary, "cs", 2, 1), coefficients(contrast_wide[1:-1]), mass_scale)
    total_field = primary + conjugate(source, None)

    surface = total_field[:, :, :, 0]
    weighted = jnp.sum(weights[:, None, None] * surface, axis=0)
    packet = jnp.concatenate([weighted.reshape(-1), electrodes.astype(jnp.float32)])
    gathered = jnp.broadcast_to(packet[None], (groups,) + packet.shape)
    if groups > 1:
        gathered = lax.all_to_all(gathered, "kq", 0, 0, tiled=True)
    if spread > 1:
        gathered = lax.all_gather(gathered, "cs")
    gathered = gathered.reshape(spread * groups, -1)
    partial = gathered[:, : sources * width].reshape(spread, groups, sources, width)
    line_surface = jnp.sum(partial, axis=1).transpose(1, 0, 2).reshape(sources, columns)
    all_electrodes = gathered[:, sources * width :].reshape(-1).astype(jnp.int32)
    count = all_electrodes.shape[0]

    picks = (all_electrodes[:, None] == jnp.arange(columns)[None, :]).astype(jnp.float32)
    potentials = jnp.sum(line_surface[:, None, :] * picks[None], axis=2)
    pole_hits = (far_pole[:, :, None] == jnp.arange(count)[None, None, :]).astype(jnp.float32)
    far_potentials = jnp.sum(potentials[:, None, :] * pole_hits, axis=2)
    predicted = potentials - far_potentials
    misfit = predicted - observed
    returned = jnp.sum(misfit[:, :, None] * pole_hits, axis=1)
    charge = misfit - returned
    own_picks = (
        all_electrodes[:, None] == offset + jnp.arange(width)[None, :]
    ).astype(jnp.float32)
    charge_cols = jnp.sum(charge[:, :, None] * own_picks[None], axis=1)
    surface_row = (jnp.arange(depth) == 0).astype(jnp.float32)
    adjoint_source = weights[:, None, None, None] * charge_cols[None, :, :, None] * surface_row
    adjoint = conjugate(adjoint_source, prior_adjoint)

    adjoint_next = next_column(adjoint, "cs")
    total_next = next_column(total_field, "cs")
    adjoint_down = jnp.concatenate([adjoint[..., 1:], jnp.zeros_like(adjoint[..., :1])], axis=-1)
    total_down = jnp.concatenate(
        [total_field[..., 1:], jnp.zeros_like(total_field[..., :1])], axis=-1
    )
    correlation = (adjoint_next - adjoint) * (total_next - total_field)
    correlation = correlation + (adjoint_down - adjoint) * (total_down - total_field)
    correlation = correlation + mass_scale * adjoint * total_field
    gradient = jnp.sum(correlation, axis=(0, 1))
    if groups > 1:
        gradient = gradient.reshape(groups, own_columns, depth)
        gradient = jnp.sum(lax.all_to_all(gradient, "kq", 0, 0, tiled=True), axis=0)
    return (predicted, gradient)


def solution(mesh):
    lines = mesh.shape["lines"]
    col = mesh.shape["col"]

    def run(*arrays):
        groups = math.gcd(col, arrays[0].shape[0])
        split = Mesh(mesh.devices.reshape(lines, col // groups, groups), ("lines", "cs", "kq"))
        cells = ("cs", "kq")
        placed = (
            P(None, "lines", cells, None),
            P(cells, "lines"),
            P(),
            P(),
            P(("lines",) + cells),
            P("lines", None),
            P("lines", None),
            P(None, "lines", cells, None),
        )
        return jax.shard_map(
            on_device,
            mesh=split,
            in_specs=placed,
            out_specs=(P("lines", None), P(cells, "lines")),
            check_vma=False,
        )(*arrays)

    return run
```

```python
import math

import jax
import jax.numpy as jnp
from jax import lax
from jax.experimental import pallas as pl
from jax.experimental.pallas import tpu as pltpu
from jax.sharding import Mesh
from jax.sharding import PartitionSpec as P

ITERS = 2
INTERPRET = False


def halo(block, axis, dim, width):
    count = lax.axis_size(axis)
    edge_shape = list(block.shape)
    edge_shape[dim] = width
    if count == 1:
        zeros = jnp.zeros(edge_shape, block.dtype)
        return jnp.concatenate([zeros, block, zeros], axis=dim)
    forward = [(i, i + 1) for i in range(count - 1)]
    backward = [(target, source) for source, target in forward]
    low = lax.ppermute(
        lax.slice_in_dim(block, block.shape[dim] - width, None, axis=dim), axis, forward
    )
    high = lax.ppermute(lax.slice_in_dim(block, 0, width, axis=dim), axis, backward)
    return jnp.concatenate([low, block, high], axis=dim)


def next_column(field, axis):
    count = lax.axis_size(axis)
    if count == 1:
        edge = jnp.zeros_like(field[:, :, :1])
    else:
        edge = lax.ppermute(field[:, :, :1], axis, [(i + 1, i) for i in range(count - 1)])
    return jnp.concatenate([field[:, :, 1:], edge], axis=2)


def coefficients(sigma_wide):
    center = sigma_wide[1:-1]
    west_face = 0.5 * (center + sigma_wide[:-2])
    east_face = 0.5 * (center + sigma_wide[2:])
    below_sigma = jnp.concatenate([center[:, 1:], jnp.zeros_like(center[:, :1])], axis=1)
    lower_face = 0.5 * (center + below_sigma)
    above_sigma = jnp.concatenate([jnp.zeros_like(center[:, :1]), center[:, :-1]], axis=1)
    upper_face = 0.5 * (center + above_sigma)
    top_row = jnp.arange(center.shape[1]) == 0
    upper_face = jnp.where(top_row[None, :], 0.0, upper_face)
    return (west_face, east_face, lower_face, upper_face, center)


def stencil(field_wide, faces_set, mass_scale):
    west_face, east_face, lower_face, upper_face, center = faces_set
    middle = field_wide[..., 1:-1, :]
    below_cells = jnp.concatenate([middle[..., 1:], jnp.zeros_like(middle[..., :1])], axis=-1)
    above_cells = jnp.concatenate([jnp.zeros_like(middle[..., :1]), middle[..., :-1]], axis=-1)
    result = west_face * (middle - field_wide[..., :-2, :]) + east_face * (
        middle - field_wide[..., 2:, :]
    )
    result = result + lower_face * (middle - below_cells) + upper_face * (middle - above_cells)
    return result + mass_scale * center * middle


def edge_shifts(field):
    rows, depth = field.shape
    row = lax.broadcasted_iota(jnp.int32, field.shape, 0)
    lane = lax.broadcasted_iota(jnp.int32, field.shape, 1)
    west = jnp.where(row == 0, 0.0, pltpu.roll(field, 1, 0))
    east = jnp.where(row == rows - 1, 0.0, pltpu.roll(field, rows - 1, 0))
    above = jnp.where(lane == 0, 0.0, pltpu.roll(field, 1, 1))
    below = jnp.where(lane == depth - 1, 0.0, pltpu.roll(field, depth - 1, 1))
    return west, east, above, below


def local_faces(center):
    west, east, above, below = edge_shifts(center)
    lane = lax.broadcasted_iota(jnp.int32, center.shape, 1)
    upper = jnp.where(lane == 0, 0.0, 0.5 * (center + above))
    return (0.5 * (center + west), 0.5 * (center + east), 0.5 * (center + below), upper, center)


def local_stencil(field, faces_set, mass_scale):
    west_face, east_face, lower_face, upper_face, center = faces_set
    west, east, above, below = edge_shifts(field)
    result = west_face * (field - west) + east_face * (field - east)
    result = result + lower_face * (field - below) + upper_face * (field - above)
    return result + mass_scale * center * field


def cell_sum(field):
    return jnp.sum(jnp.sum(field, axis=1, keepdims=True), axis=0, keepdims=True)


def local_conjugate(source, start, operate):
    if start is None:
        solution = jnp.zeros_like(source)
        residual = source
    else:
        solution = start
        residual = source - operate(start)
    direction = residual
    norm_now = cell_sum(residual * residual)
    for iteration in range(ITERS):
        applied = operate(direction)
        step_size = norm_now / cell_sum(direction * applied)
        solution = solution + step_size * direction
        if iteration + 1 < ITERS:
            residual = residual - step_size * applied
            norm_next = cell_sum(residual * residual)
            direction = residual + (norm_next / norm_now) * direction
            norm_now = norm_next
    return solution


def forward_kernel(scale_ref, primary_ref, sigma_ref, total_ref):
    sigma = sigma_ref[...]
    operator_faces = local_faces(sigma)
    contrast_faces = local_faces(sigma - 1.0)
    for field in range(primary_ref.shape[0]):
        mass_scale = scale_ref[field]
        primary = primary_ref[field]
        source = -local_stencil(primary, contrast_faces, mass_scale)
        secondary = local_conjugate(
            source, None, lambda state: local_stencil(state, operator_faces, mass_scale)
        )
        total_ref[field] = primary + secondary


def adjoint_kernel(scale_ref, charge_ref, total_ref, prior_ref, sigma_ref, gradient_ref):
    sigma = sigma_ref[...]
    operator_faces = local_faces(sigma)
    lane = lax.broadcasted_iota(jnp.int32, sigma.shape, 1)
    surface_row = (lane == 0).astype(jnp.float32)
    gradient = jnp.zeros_like(sigma)
    for field in range(prior_ref.shape[0]):
        mass_scale = scale_ref[field]
        adjoint_source = charge_ref[field] * surface_row
        adjoint = local_conjugate(
            adjoint_source,
            prior_ref[field],
            lambda state: local_stencil(state, operator_faces, mass_scale),
        )
        total_field = total_ref[field]
        unused, adjoint_next, unused, adjoint_down = edge_shifts(adjoint)
        unused, total_next, unused, total_down = edge_shifts(total_field)
        correlation = (adjoint_next - adjoint) * (total_next - total_field)
        correlation = correlation + (adjoint_down - adjoint) * (total_down - total_field)
        correlation = correlation + mass_scale * adjoint * total_field
        gradient = gradient + correlation
    gradient_ref[...] = gradient


def vmem_spec():
    return pl.BlockSpec(memory_space=pltpu.MemorySpace.VMEM)


def smem_spec():
    return pl.BlockSpec(memory_space=pltpu.MemorySpace.SMEM)


def forward_call(scales, primary, sigma):
    return pl.pallas_call(
        forward_kernel,
        out_shape=jax.ShapeDtypeStruct(primary.shape, jnp.float32),
        in_specs=[smem_spec(), vmem_spec(), vmem_spec()],
        out_specs=vmem_spec(),
        interpret=INTERPRET,
    )(scales, primary, sigma)


def adjoint_call(scales, charge, total_field, prior, sigma):
    return pl.pallas_call(
        adjoint_kernel,
        out_shape=jax.ShapeDtypeStruct(sigma.shape, jnp.float32),
        in_specs=[smem_spec()] + [vmem_spec()] * 4,
        out_specs=vmem_spec(),
        interpret=INTERPRET,
    )(scales, charge, total_field, prior, sigma)


def on_device(
    primary, conductivity, wavenumbers, quadrature, electrodes, far_pole, observed, prior_adjoint
):
    groups = lax.axis_size("kq")
    spread = lax.axis_size("cs")
    waves, sources, own_columns, depth = primary.shape
    per_group = waves // groups
    group = lax.axis_index("kq")
    block = lax.axis_index("cs")
    fields = per_group * sources

    def by_group(array):
        return array.reshape(groups, fields, own_columns, depth)

    sigma_copies = jnp.broadcast_to(conductivity[None, None], (groups, 1, own_columns, depth))
    send = jnp.concatenate([by_group(primary), by_group(prior_adjoint), sigma_copies], axis=1)
    if groups > 1:
        send = lax.all_to_all(send, "kq", 0, 2, tiled=True)
    received = send[0]
    width = groups * own_columns
    primary = received[:fields].reshape(per_group, sources, width, depth)
    prior_adjoint = received[fields : 2 * fields].reshape(per_group, sources, width, depth)
    sigma = received[2 * fields]

    columns = width * spread
    offset = block * width
    wide_sigma = halo(sigma, "cs", 0, 2)
    positions = offset - 2 + jnp.arange(width + 4)
    inside = (positions >= 0) & (positions < columns)
    contrast_wide = jnp.where(inside[:, None], wide_sigma - 1.0, 0.0)
    own_waves = lax.dynamic_slice_in_dim(wavenumbers, group * per_group, per_group)
    weights = lax.dynamic_slice_in_dim(quadrature, group * per_group, per_group)
    mass_scale = (own_waves * own_waves)[:, None, None, None]
    operator_faces = coefficients(wide_sigma[1:-1])

    def operate(state):
        return stencil(halo(state, "cs", 2, 1), operator_faces, mass_scale)

    def dots(left, right):
        total = jnp.sum(left * right, axis=(2, 3))
        if spread > 1:
            total = lax.psum(total, "cs")
        return total[:, :, None, None]

    def conjugate(source, start):
        if start is None:
            solution = jnp.zeros_like(source)
            residual = source
        else:
            solution = start
            residual = source - operate(start)
        direction = residual
        norm_now = dots(residual, residual)
        for iteration in range(ITERS):
            applied = operate(direction)
            step_size = norm_now / dots(direction, applied)
            solution = solution + step_size * direction
            if iteration + 1 < ITERS:
                residual = residual - step_size * applied
                norm_next = dots(residual, residual)
                direction = residual + (norm_next / norm_now) * direction
                norm_now = norm_next
        return solution

    scales = jnp.repeat(own_waves * own_waves, sources)
    if spread == 1:
        flat = (fields, width, depth)
        total_field = forward_call(scales, primary.reshape(flat), sigma).reshape(primary.shape)
    else:
        source = -stencil(
            halo(primary, "cs", 2, 1), coefficients(contrast_wide[1:-1]), mass_scale
        )
        total_field = primary + conjugate(source, None)

    surface = total_field[:, :, :, 0]
    weighted = jnp.sum(weights[:, None, None] * surface, axis=0)
    packet = jnp.concatenate([weighted.reshape(-1), electrodes.astype(jnp.float32)])
    gathered = jnp.broadcast_to(packet[None], (groups,) + packet.shape)
    if groups > 1:
        gathered = lax.all_to_all(gathered, "kq", 0, 0, tiled=True)
    if spread > 1:
        gathered = lax.all_gather(gathered, "cs")
    gathered = gathered.reshape(spread * groups, -1)
    partial = gathered[:, : sources * width].reshape(spread, groups, sources, width)
    line_surface = jnp.sum(partial, axis=1).transpose(1, 0, 2).reshape(sources, columns)
    all_electrodes = gathered[:, sources * width :].reshape(-1).astype(jnp.int32)
    count = all_electrodes.shape[0]

    picks = (all_electrodes[:, None] == jnp.arange(columns)[None, :]).astype(jnp.float32)
    potentials = jnp.sum(line_surface[:, None, :] * picks[None], axis=2)
    pole_hits = (far_pole[:, :, None] == jnp.arange(count)[None, None, :]).astype(jnp.float32)
    far_potentials = jnp.sum(potentials[:, None, :] * pole_hits, axis=2)
    predicted = potentials - far_potentials
    misfit = predicted - observed
    returned = jnp.sum(misfit[:, :, None] * pole_hits, axis=1)
    charge = misfit - returned
    own_picks = (
        all_electrodes[:, None] == offset + jnp.arange(width)[None, :]
    ).astype(jnp.float32)
    charge_cols = jnp.sum(charge[:, :, None] * own_picks[None], axis=1)
    if spread == 1:
        charge_field = (weights[:, None, None] * charge_cols[None]).reshape(fields, width, 1)
        gradient = adjoint_call(
            scales, charge_field, total_field.reshape(flat), prior_adjoint.reshape(flat), sigma
        )
    else:
        surface_row = (jnp.arange(depth) == 0).astype(jnp.float32)
        adjoint_source = weights[:, None, None, None] * charge_cols[None, :, :, None] * surface_row
        adjoint = conjugate(adjoint_source, prior_adjoint)
        adjoint_next = next_column(adjoint, "cs")
        total_next = next_column(total_field, "cs")
        adjoint_down = jnp.concatenate(
            [adjoint[..., 1:], jnp.zeros_like(adjoint[..., :1])], axis=-1
        )
        total_down = jnp.concatenate(
            [total_field[..., 1:], jnp.zeros_like(total_field[..., :1])], axis=-1
        )
        correlation = (adjoint_next - adjoint) * (total_next - total_field)
        correlation = correlation + (adjoint_down - adjoint) * (total_down - total_field)
        correlation = correlation + mass_scale * adjoint * total_field
        gradient = jnp.sum(correlation, axis=(0, 1))
    if groups > 1:
        gradient = gradient.reshape(groups, own_columns, depth)
        gradient = jnp.sum(lax.all_to_all(gradient, "kq", 0, 0, tiled=True), axis=0)
    return (predicted, gradient)


def solution(mesh):
    lines = mesh.shape["lines"]
    col = mesh.shape["col"]

    def run(*arrays):
        groups = math.gcd(col, arrays[0].shape[0])
        split = Mesh(mesh.devices.reshape(lines, col // groups, groups), ("lines", "cs", "kq"))
        cells = ("cs", "kq")
        placed = (
            P(None, "lines", cells, None),
            P(cells, "lines"),
            P(),
            P(),
            P(("lines",) + cells),
            P("lines", None),
            P("lines", None),
            P(None, "lines", cells, None),
        )
        return jax.shard_map(
            on_device,
            mesh=split,
            in_specs=placed,
            out_specs=(P("lines", None), P(cells, "lines")),
            check_vma=False,
        )(*arrays)

    return run
```

```python
import math

import jax
import jax.numpy as jnp
from jax import lax
from jax.experimental import pallas as pl
from jax.experimental.pallas import tpu as pltpu
from jax.sharding import Mesh
from jax.sharding import PartitionSpec as P

ITERS = 2
INTERPRET = False


def halo(block, axis, dim, width):
    count = lax.axis_size(axis)
    edge_shape = list(block.shape)
    edge_shape[dim] = width
    if count == 1:
        zeros = jnp.zeros(edge_shape, block.dtype)
        return jnp.concatenate([zeros, block, zeros], axis=dim)
    forward = [(i, i + 1) for i in range(count - 1)]
    backward = [(target, source) for source, target in forward]
    low = lax.ppermute(
        lax.slice_in_dim(block, block.shape[dim] - width, None, axis=dim), axis, forward
    )
    high = lax.ppermute(lax.slice_in_dim(block, 0, width, axis=dim), axis, backward)
    return jnp.concatenate([low, block, high], axis=dim)


def next_column(field, axis):
    count = lax.axis_size(axis)
    if count == 1:
        edge = jnp.zeros_like(field[:, :, :1])
    else:
        edge = lax.ppermute(field[:, :, :1], axis, [(i + 1, i) for i in range(count - 1)])
    return jnp.concatenate([field[:, :, 1:], edge], axis=2)


def coefficients(sigma_wide):
    center = sigma_wide[1:-1]
    west_face = 0.5 * (center + sigma_wide[:-2])
    east_face = 0.5 * (center + sigma_wide[2:])
    below_sigma = jnp.concatenate([center[:, 1:], jnp.zeros_like(center[:, :1])], axis=1)
    lower_face = 0.5 * (center + below_sigma)
    above_sigma = jnp.concatenate([jnp.zeros_like(center[:, :1]), center[:, :-1]], axis=1)
    upper_face = 0.5 * (center + above_sigma)
    top_row = jnp.arange(center.shape[1]) == 0
    upper_face = jnp.where(top_row[None, :], 0.0, upper_face)
    return (west_face, east_face, lower_face, upper_face, center)


def stencil(field_wide, faces_set, mass_scale):
    west_face, east_face, lower_face, upper_face, center = faces_set
    middle = field_wide[..., 1:-1, :]
    below_cells = jnp.concatenate([middle[..., 1:], jnp.zeros_like(middle[..., :1])], axis=-1)
    above_cells = jnp.concatenate([jnp.zeros_like(middle[..., :1]), middle[..., :-1]], axis=-1)
    result = west_face * (middle - field_wide[..., :-2, :]) + east_face * (
        middle - field_wide[..., 2:, :]
    )
    result = result + lower_face * (middle - below_cells) + upper_face * (middle - above_cells)
    return result + mass_scale * center * middle


def pack_kernel(primary_ref, prior_ref, sigma_ref, send_ref, flags):
    groups, fields = primary_ref.shape[:2]
    copies = [
        pltpu.make_async_copy(primary_ref, send_ref.at[:, 0:fields], flags.at[0]),
        pltpu.make_async_copy(prior_ref, send_ref.at[:, fields : 2 * fields], flags.at[1]),
    ]
    for target in range(groups):
        copies.append(
            pltpu.make_async_copy(
                sigma_ref, send_ref.at[target, 2 * fields], flags.at[2 + target]
            )
        )
    for copy in copies:
        copy.start()
    for copy in copies:
        copy.wait()


def pack(primary, prior, sigma):
    groups, fields, rows, depth = primary.shape
    anywhere = pl.BlockSpec(memory_space=pl.ANY)
    return pl.pallas_call(
        pack_kernel,
        out_shape=jax.ShapeDtypeStruct((groups, 2 * fields + 1, rows, depth), jnp.float32),
        in_specs=[anywhere] * 3,
        out_specs=anywhere,
        scratch_shapes=[pltpu.SemaphoreType.DMA((groups + 2,))],
        interpret=INTERPRET,
    )(primary, prior, sigma)


def on_device(
    primary, conductivity, wavenumbers, quadrature, electrodes, far_pole, observed, prior_adjoint
):
    groups = lax.axis_size("kq")
    spread = lax.axis_size("cs")
    waves, sources, own_columns, depth = primary.shape
    per_group = waves // groups
    group = lax.axis_index("kq")
    block = lax.axis_index("cs")
    fields = per_group * sources

    def by_group(array):
        return array.reshape(groups, fields, own_columns, depth)

    send = pack(by_group(primary), by_group(prior_adjoint), conductivity)
    if groups > 1:
        send = lax.all_to_all(send, "kq", 0, 2, tiled=True)
    received = send[0]
    width = groups * own_columns
    primary = received[:fields].reshape(per_group, sources, width, depth)
    prior_adjoint = received[fields : 2 * fields].reshape(per_group, sources, width, depth)
    sigma = received[2 * fields]

    columns = width * spread
    offset = block * width
    wide_sigma = halo(sigma, "cs", 0, 2)
    positions = offset - 2 + jnp.arange(width + 4)
    inside = (positions >= 0) & (positions < columns)
    contrast_wide = jnp.where(inside[:, None], wide_sigma - 1.0, 0.0)
    own_waves = lax.dynamic_slice_in_dim(wavenumbers, group * per_group, per_group)
    weights = lax.dynamic_slice_in_dim(quadrature, group * per_group, per_group)
    mass_scale = (own_waves * own_waves)[:, None, None, None]
    operator_faces = coefficients(wide_sigma[1:-1])

    def operate(state):
        return stencil(halo(state, "cs", 2, 1), operator_faces, mass_scale)

    def dots(left, right):
        total = jnp.sum(left * right, axis=(2, 3))
        if spread > 1:
            total = lax.psum(total, "cs")
        return total[:, :, None, None]

    def conjugate(source, start):
        if start is None:
            solution = jnp.zeros_like(source)
            residual = source
        else:
            solution = start
            residual = source - operate(start)
        direction = residual
        norm_now = dots(residual, residual)
        for iteration in range(ITERS):
            applied = operate(direction)
            step_size = norm_now / dots(direction, applied)
            solution = solution + step_size * direction
            if iteration + 1 < ITERS:
                residual = residual - step_size * applied
                norm_next = dots(residual, residual)
                direction = residual + (norm_next / norm_now) * direction
                norm_now = norm_next
        return solution

    source = -stencil(halo(primary, "cs", 2, 1), coefficients(contrast_wide[1:-1]), mass_scale)
    total_field = primary + conjugate(source, None)

    surface = total_field[:, :, :, 0]
    weighted = jnp.sum(weights[:, None, None] * surface, axis=0)
    packet = jnp.concatenate([weighted.reshape(-1), electrodes.astype(jnp.float32)])
    gathered = jnp.broadcast_to(packet[None], (groups,) + packet.shape)
    if groups > 1:
        gathered = lax.all_to_all(gathered, "kq", 0, 0, tiled=True)
    if spread > 1:
        gathered = lax.all_gather(gathered, "cs")
    gathered = gathered.reshape(spread * groups, -1)
    partial = gathered[:, : sources * width].reshape(spread, groups, sources, width)
    line_surface = jnp.sum(partial, axis=1).transpose(1, 0, 2).reshape(sources, columns)
    all_electrodes = gathered[:, sources * width :].reshape(-1).astype(jnp.int32)
    count = all_electrodes.shape[0]

    picks = (all_electrodes[:, None] == jnp.arange(columns)[None, :]).astype(jnp.float32)
    potentials = jnp.sum(line_surface[:, None, :] * picks[None], axis=2)
    pole_hits = (far_pole[:, :, None] == jnp.arange(count)[None, None, :]).astype(jnp.float32)
    far_potentials = jnp.sum(potentials[:, None, :] * pole_hits, axis=2)
    predicted = potentials - far_potentials
    misfit = predicted - observed
    returned = jnp.sum(misfit[:, :, None] * pole_hits, axis=1)
    charge = misfit - returned
    own_picks = (
        all_electrodes[:, None] == offset + jnp.arange(width)[None, :]
    ).astype(jnp.float32)
    charge_cols = jnp.sum(charge[:, :, None] * own_picks[None], axis=1)
    surface_row = (jnp.arange(depth) == 0).astype(jnp.float32)
    adjoint_source = weights[:, None, None, None] * charge_cols[None, :, :, None] * surface_row
    adjoint = conjugate(adjoint_source, prior_adjoint)

    adjoint_next = next_column(adjoint, "cs")
    total_next = next_column(total_field, "cs")
    adjoint_down = jnp.concatenate([adjoint[..., 1:], jnp.zeros_like(adjoint[..., :1])], axis=-1)
    total_down = jnp.concatenate(
        [total_field[..., 1:], jnp.zeros_like(total_field[..., :1])], axis=-1
    )
    correlation = (adjoint_next - adjoint) * (total_next - total_field)
    correlation = correlation + (adjoint_down - adjoint) * (total_down - total_field)
    correlation = correlation + mass_scale * adjoint * total_field
    gradient = jnp.sum(correlation, axis=(0, 1))
    if groups > 1:
        gradient = gradient.reshape(groups, own_columns, depth)
        gradient = jnp.sum(lax.all_to_all(gradient, "kq", 0, 0, tiled=True), axis=0)
    return (predicted, gradient)


def solution(mesh):
    lines = mesh.shape["lines"]
    col = mesh.shape["col"]

    def run(*arrays):
        groups = math.gcd(col, arrays[0].shape[0])
        split = Mesh(mesh.devices.reshape(lines, col // groups, groups), ("lines", "cs", "kq"))
        cells = ("cs", "kq")
        placed = (
            P(None, "lines", cells, None),
            P(cells, "lines"),
            P(),
            P(),
            P(("lines",) + cells),
            P("lines", None),
            P("lines", None),
            P(None, "lines", cells, None),
        )
        return jax.shard_map(
            on_device,
            mesh=split,
            in_specs=placed,
            out_specs=(P("lines", None), P(cells, "lines")),
            check_vma=False,
        )(*arrays)

    return run
```

```python
import math

import jax
import jax.numpy as jnp
from jax import lax
from jax.experimental import pallas as pl
from jax.experimental.pallas import tpu as pltpu
from jax.sharding import Mesh
from jax.sharding import PartitionSpec as P

ITERS = 2


def halo(block, axis, dim, width):
    count = lax.axis_size(axis)
    edge_shape = list(block.shape)
    edge_shape[dim] = width
    if count == 1:
        zeros = jnp.zeros(edge_shape, block.dtype)
        return jnp.concatenate([zeros, block, zeros], axis=dim)
    forward = [(i, i + 1) for i in range(count - 1)]
    backward = [(target, source) for source, target in forward]
    low = lax.ppermute(
        lax.slice_in_dim(block, block.shape[dim] - width, None, axis=dim), axis, forward
    )
    high = lax.ppermute(lax.slice_in_dim(block, 0, width, axis=dim), axis, backward)
    return jnp.concatenate([low, block, high], axis=dim)


def next_column(field, axis):
    count = lax.axis_size(axis)
    if count == 1:
        edge = jnp.zeros_like(field[:, :, :1])
    else:
        edge = lax.ppermute(field[:, :, :1], axis, [(i + 1, i) for i in range(count - 1)])
    return jnp.concatenate([field[:, :, 1:], edge], axis=2)


def coefficients(sigma_wide):
    center = sigma_wide[1:-1]
    west_face = 0.5 * (center + sigma_wide[:-2])
    east_face = 0.5 * (center + sigma_wide[2:])
    below_sigma = jnp.concatenate([center[:, 1:], jnp.zeros_like(center[:, :1])], axis=1)
    lower_face = 0.5 * (center + below_sigma)
    above_sigma = jnp.concatenate([jnp.zeros_like(center[:, :1]), center[:, :-1]], axis=1)
    upper_face = 0.5 * (center + above_sigma)
    top_row = jnp.arange(center.shape[1]) == 0
    upper_face = jnp.where(top_row[None, :], 0.0, upper_face)
    return (west_face, east_face, lower_face, upper_face, center)


def stencil(field_wide, faces_set, mass_scale):
    west_face, east_face, lower_face, upper_face, center = faces_set
    middle = field_wide[..., 1:-1, :]
    below_cells = jnp.concatenate([middle[..., 1:], jnp.zeros_like(middle[..., :1])], axis=-1)
    above_cells = jnp.concatenate([jnp.zeros_like(middle[..., :1]), middle[..., :-1]], axis=-1)
    result = west_face * (middle - field_wide[..., :-2, :]) + east_face * (
        middle - field_wide[..., 2:, :]
    )
    result = result + lower_face * (middle - below_cells) + upper_face * (middle - above_cells)
    return result + mass_scale * center * middle


def pack_kernel(primary_ref, prior_ref, sigma_ref, send_ref):
    fields = primary_ref.shape[1]
    send_ref[:, 0:fields] = primary_ref[...]
    send_ref[:, fields : 2 * fields] = prior_ref[...]
    sigma = sigma_ref[...]
    for target in range(send_ref.shape[0]):
        send_ref[target, 2 * fields] = sigma


def pack(primary, prior, sigma):
    groups, fields, rows, depth = primary.shape
    vmem = pl.BlockSpec(memory_space=pltpu.MemorySpace.VMEM)
    return pl.pallas_call(
        pack_kernel,
        out_shape=jax.ShapeDtypeStruct((groups, 2 * fields + 1, rows, depth), jnp.float32),
        in_specs=[vmem] * 3,
        out_specs=vmem,
    )(primary, prior, sigma)


def on_device(
    primary, conductivity, wavenumbers, quadrature, electrodes, far_pole, observed, prior_adjoint
):
    groups = lax.axis_size("kq")
    spread = lax.axis_size("cs")
    waves, sources, own_columns, depth = primary.shape
    per_group = waves // groups
    group = lax.axis_index("kq")
    block = lax.axis_index("cs")
    fields = per_group * sources

    def by_group(array):
        return array.reshape(groups, fields, own_columns, depth)

    send = pack(by_group(primary), by_group(prior_adjoint), conductivity)
    if groups > 1:
        send = lax.all_to_all(send, "kq", 0, 2, tiled=True)
    received = send[0]
    width = groups * own_columns
    primary = received[:fields].reshape(per_group, sources, width, depth)
    prior_adjoint = received[fields : 2 * fields].reshape(per_group, sources, width, depth)
    sigma = received[2 * fields]

    columns = width * spread
    offset = block * width
    wide_sigma = halo(sigma, "cs", 0, 2)
    positions = offset - 2 + jnp.arange(width + 4)
    inside = (positions >= 0) & (positions < columns)
    contrast_wide = jnp.where(inside[:, None], wide_sigma - 1.0, 0.0)
    own_waves = lax.dynamic_slice_in_dim(wavenumbers, group * per_group, per_group)
    weights = lax.dynamic_slice_in_dim(quadrature, group * per_group, per_group)
    mass_scale = (own_waves * own_waves)[:, None, None, None]
    operator_faces = coefficients(wide_sigma[1:-1])

    def operate(state):
        return stencil(halo(state, "cs", 2, 1), operator_faces, mass_scale)

    def dots(left, right):
        total = jnp.sum(left * right, axis=(2, 3))
        if spread > 1:
            total = lax.psum(total, "cs")
        return total[:, :, None, None]

    def conjugate(source, start):
        if start is None:
            solution = jnp.zeros_like(source)
            residual = source
        else:
            solution = start
            residual = source - operate(start)
        direction = residual
        norm_now = dots(residual, residual)
        for iteration in range(ITERS):
            applied = operate(direction)
            step_size = norm_now / dots(direction, applied)
            solution = solution + step_size * direction
            if iteration + 1 < ITERS:
                residual = residual - step_size * applied
                norm_next = dots(residual, residual)
                direction = residual + (norm_next / norm_now) * direction
                norm_now = norm_next
        return solution

    source = -stencil(halo(primary, "cs", 2, 1), coefficients(contrast_wide[1:-1]), mass_scale)
    total_field = primary + conjugate(source, None)

    surface = total_field[:, :, :, 0]
    weighted = jnp.sum(weights[:, None, None] * surface, axis=0)
    packet = jnp.concatenate([weighted.reshape(-1), electrodes.astype(jnp.float32)])
    pole_hits = (far_pole[:, :, None] == jnp.arange(far_pole.shape[1])[None, None, :]).astype(jnp.float32)
    packet, pole_hits, observed = lax.optimization_barrier((packet, pole_hits, observed))
    gathered = jnp.broadcast_to(packet[None], (groups,) + packet.shape)
    if groups > 1:
        gathered = lax.all_to_all(gathered, "kq", 0, 0, tiled=True)
    if spread > 1:
        gathered = lax.all_gather(gathered, "cs")
    gathered = gathered.reshape(spread * groups, -1)
    partial = gathered[:, : sources * width].reshape(spread, groups, sources, width)
    line_surface = jnp.sum(partial, axis=1).transpose(1, 0, 2).reshape(sources, columns)
    all_electrodes = gathered[:, sources * width :].reshape(-1).astype(jnp.int32)
    count = all_electrodes.shape[0]

    picks = (all_electrodes[:, None] == jnp.arange(columns)[None, :]).astype(jnp.float32)
    potentials = jnp.sum(line_surface[:, None, :] * picks[None], axis=2)
    far_potentials = jnp.sum(potentials[:, None, :] * pole_hits, axis=2)
    predicted = potentials - far_potentials
    misfit = predicted - observed
    returned = jnp.sum(misfit[:, :, None] * pole_hits, axis=1)
    charge = misfit - returned
    own_picks = (
        all_electrodes[:, None] == offset + jnp.arange(width)[None, :]
    ).astype(jnp.float32)
    charge_cols = jnp.sum(charge[:, :, None] * own_picks[None], axis=1)
    surface_row = (jnp.arange(depth) == 0).astype(jnp.float32)
    adjoint_source = weights[:, None, None, None] * charge_cols[None, :, :, None] * surface_row
    adjoint = conjugate(adjoint_source, prior_adjoint)

    adjoint_next = next_column(adjoint, "cs")
    total_next = next_column(total_field, "cs")
    adjoint_down = jnp.concatenate([adjoint[..., 1:], jnp.zeros_like(adjoint[..., :1])], axis=-1)
    total_down = jnp.concatenate(
        [total_field[..., 1:], jnp.zeros_like(total_field[..., :1])], axis=-1
    )
    correlation = (adjoint_next - adjoint) * (total_next - total_field)
    correlation = correlation + (adjoint_down - adjoint) * (total_down - total_field)
    correlation = correlation + mass_scale * adjoint * total_field
    gradient = jnp.sum(correlation, axis=(0, 1))
    if groups > 1:
        gradient = gradient.reshape(groups, own_columns, depth)
        gradient = jnp.sum(lax.all_to_all(gradient, "kq", 0, 0, tiled=True), axis=0)
    return (predicted, gradient)


def solution(mesh):
    lines = mesh.shape["lines"]
    col = mesh.shape["col"]

    def run(*arrays):
        groups = math.gcd(col, arrays[0].shape[0])
        split = Mesh(mesh.devices.reshape(lines, col // groups, groups), ("lines", "cs", "kq"))
        cells = ("cs", "kq")
        placed = (
            P(None, "lines", cells, None),
            P(cells, "lines"),
            P(),
            P(),
            P(("lines",) + cells),
            P("lines", None),
            P("lines", None),
            P(None, "lines", cells, None),
        )
        return jax.shard_map(
            on_device,
            mesh=split,
            in_specs=placed,
            out_specs=(P("lines", None), P(cells, "lines")),
            check_vma=False,
        )(*arrays)

    return run
```

```python
import math

import jax
import jax.numpy as jnp
from jax import lax
from jax.experimental import pallas as pl
from jax.experimental.pallas import tpu as pltpu
from jax.sharding import Mesh
from jax.sharding import PartitionSpec as P

ITERS = 2
INTERPRET = False


def halo(block, axis, dim, width):
    count = lax.axis_size(axis)
    edge_shape = list(block.shape)
    edge_shape[dim] = width
    if count == 1:
        zeros = jnp.zeros(edge_shape, block.dtype)
        return jnp.concatenate([zeros, block, zeros], axis=dim)
    forward = [(i, i + 1) for i in range(count - 1)]
    backward = [(target, source) for source, target in forward]
    low = lax.ppermute(
        lax.slice_in_dim(block, block.shape[dim] - width, None, axis=dim), axis, forward
    )
    high = lax.ppermute(lax.slice_in_dim(block, 0, width, axis=dim), axis, backward)
    return jnp.concatenate([low, block, high], axis=dim)


def next_column(field, axis):
    count = lax.axis_size(axis)
    if count == 1:
        edge = jnp.zeros_like(field[:, :, :1])
    else:
        edge = lax.ppermute(field[:, :, :1], axis, [(i + 1, i) for i in range(count - 1)])
    return jnp.concatenate([field[:, :, 1:], edge], axis=2)


def coefficients(sigma_wide):
    center = sigma_wide[1:-1]
    west_face = 0.5 * (center + sigma_wide[:-2])
    east_face = 0.5 * (center + sigma_wide[2:])
    below_sigma = jnp.concatenate([center[:, 1:], jnp.zeros_like(center[:, :1])], axis=1)
    lower_face = 0.5 * (center + below_sigma)
    above_sigma = jnp.concatenate([jnp.zeros_like(center[:, :1]), center[:, :-1]], axis=1)
    upper_face = 0.5 * (center + above_sigma)
    top_row = jnp.arange(center.shape[1]) == 0
    upper_face = jnp.where(top_row[None, :], 0.0, upper_face)
    return (west_face, east_face, lower_face, upper_face, center)


def stencil(field_wide, faces_set, mass_scale):
    west_face, east_face, lower_face, upper_face, center = faces_set
    middle = field_wide[..., 1:-1, :]
    below_cells = jnp.concatenate([middle[..., 1:], jnp.zeros_like(middle[..., :1])], axis=-1)
    above_cells = jnp.concatenate([jnp.zeros_like(middle[..., :1]), middle[..., :-1]], axis=-1)
    result = west_face * (middle - field_wide[..., :-2, :]) + east_face * (
        middle - field_wide[..., 2:, :]
    )
    result = result + lower_face * (middle - below_cells) + upper_face * (middle - above_cells)
    return result + mass_scale * center * middle


def pack_kernel(primary_ref, prior_ref, sigma_ref, send_ref):
    fields = primary_ref.shape[1]
    send_ref[:, 0:fields] = primary_ref[...]
    send_ref[:, fields : 2 * fields] = prior_ref[...]
    sigma = sigma_ref[...]
    for target in range(send_ref.shape[0]):
        send_ref[target, 2 * fields] = sigma


def pack(primary, prior, sigma):
    groups, fields, rows, depth = primary.shape
    steps = 2 if groups % 2 == 0 else 1
    chunk = groups // steps
    part = pl.BlockSpec((chunk, fields, rows, depth), lambda i: (i, 0, 0, 0))
    return pl.pallas_call(
        pack_kernel,
        out_shape=jax.ShapeDtypeStruct((groups, 2 * fields + 1, rows, depth), jnp.float32),
        grid=(steps,),
        in_specs=[part, part, pl.BlockSpec((rows, depth), lambda i: (0, 0))],
        out_specs=pl.BlockSpec((chunk, 2 * fields + 1, rows, depth), lambda i: (i, 0, 0, 0)),
        interpret=INTERPRET,
    )(primary, prior, sigma)

def on_device(
    primary, conductivity, wavenumbers, quadrature, electrodes, far_pole, observed, prior_adjoint
):
    groups = lax.axis_size("kq")
    spread = lax.axis_size("cs")
    waves, sources, own_columns, depth = primary.shape
    per_group = waves // groups
    group = lax.axis_index("kq")
    block = lax.axis_index("cs")
    fields = per_group * sources

    def by_group(array):
        return array.reshape(groups, fields, own_columns, depth)

    send = pack(by_group(primary), by_group(prior_adjoint), conductivity)
    if groups > 1:
        send = lax.all_to_all(send, "kq", 0, 2, tiled=True)
    received = send[0]
    width = groups * own_columns
    primary = received[:fields].reshape(per_group, sources, width, depth)
    prior_adjoint = received[fields : 2 * fields].reshape(per_group, sources, width, depth)
    sigma = received[2 * fields]

    columns = width * spread
    offset = block * width
    wide_sigma = halo(sigma, "cs", 0, 2)
    positions = offset - 2 + jnp.arange(width + 4)
    inside = (positions >= 0) & (positions < columns)
    contrast_wide = jnp.where(inside[:, None], wide_sigma - 1.0, 0.0)
    own_waves = lax.dynamic_slice_in_dim(wavenumbers, group * per_group, per_group)
    weights = lax.dynamic_slice_in_dim(quadrature, group * per_group, per_group)
    mass_scale = (own_waves * own_waves)[:, None, None, None]
    operator_faces = coefficients(wide_sigma[1:-1])

    def operate(state):
        return stencil(halo(state, "cs", 2, 1), operator_faces, mass_scale)

    def dots(left, right):
        total = jnp.sum(left * right, axis=(2, 3))
        if spread > 1:
            total = lax.psum(total, "cs")
        return total[:, :, None, None]

    def conjugate(source, start):
        if start is None:
            solution = jnp.zeros_like(source)
            residual = source
        else:
            solution = start
            residual = source - operate(start)
        direction = residual
        norm_now = dots(residual, residual)
        for iteration in range(ITERS):
            applied = operate(direction)
            step_size = norm_now / dots(direction, applied)
            solution = solution + step_size * direction
            if iteration + 1 < ITERS:
                residual = residual - step_size * applied
                norm_next = dots(residual, residual)
                direction = residual + (norm_next / norm_now) * direction
                norm_now = norm_next
        return solution

    source = -stencil(halo(primary, "cs", 2, 1), coefficients(contrast_wide[1:-1]), mass_scale)
    total_field = primary + conjugate(source, None)

    surface = total_field[:, :, :, 0]
    weighted = jnp.sum(weights[:, None, None] * surface, axis=0)
    packet = jnp.concatenate([weighted.reshape(-1), electrodes.astype(jnp.float32)])
    pole_hits = (far_pole[:, :, None] == jnp.arange(far_pole.shape[1])[None, None, :]).astype(jnp.float32)
    packet, pole_hits, held = lax.optimization_barrier((packet, pole_hits, 0.0 - observed))
    gathered = jnp.broadcast_to(packet[None], (groups,) + packet.shape)
    if groups > 1:
        gathered = lax.all_to_all(gathered, "kq", 0, 0)
    if spread > 1:
        gathered = lax.all_gather(gathered, "cs")
    gathered = gathered.reshape(spread * groups, -1)
    partial = gathered[:, : sources * width].reshape(spread, groups, sources, width)
    line_surface = jnp.sum(partial, axis=1).transpose(1, 0, 2).reshape(sources, columns)
    all_electrodes = gathered[:, sources * width :].reshape(-1).astype(jnp.int32)
    count = all_electrodes.shape[0]

    picks = (all_electrodes[:, None] == jnp.arange(columns)[None, :]).astype(jnp.float32)
    potentials = jnp.sum(line_surface[:, None, :] * picks[None], axis=2)
    far_potentials = jnp.sum(potentials[:, None, :] * pole_hits, axis=2)
    predicted = potentials - far_potentials
    misfit = predicted + held
    returned = jnp.sum(misfit[:, :, None] * pole_hits, axis=1)
    charge = misfit - returned
    own_picks = (
        all_electrodes[:, None] == offset + jnp.arange(width)[None, :]
    ).astype(jnp.float32)
    charge_cols = jnp.sum(charge[:, :, None] * own_picks[None], axis=1)
    surface_row = (jnp.arange(depth) == 0).astype(jnp.float32)
    adjoint_source = weights[:, None, None, None] * charge_cols[None, :, :, None] * surface_row
    adjoint = conjugate(adjoint_source, prior_adjoint)

    adjoint_next = next_column(adjoint, "cs")
    total_next = next_column(total_field, "cs")
    adjoint_down = jnp.concatenate([adjoint[..., 1:], jnp.zeros_like(adjoint[..., :1])], axis=-1)
    total_down = jnp.concatenate(
        [total_field[..., 1:], jnp.zeros_like(total_field[..., :1])], axis=-1
    )
    correlation = (adjoint_next - adjoint) * (total_next - total_field)
    correlation = correlation + (adjoint_down - adjoint) * (total_down - total_field)
    correlation = correlation + mass_scale * adjoint * total_field
    gradient = jnp.sum(correlation, axis=(0, 1))
    if groups > 1:
        gradient = gradient.reshape(groups, own_columns, depth)
        gradient = jnp.sum(lax.all_to_all(gradient, "kq", 0, 0, tiled=True), axis=0)
    return (predicted, gradient)


def solution(mesh):
    lines = mesh.shape["lines"]
    col = mesh.shape["col"]

    def run(*arrays):
        groups = math.gcd(col, arrays[0].shape[0])
        split = Mesh(mesh.devices.reshape(lines, col // groups, groups), ("lines", "cs", "kq"))
        cells = ("cs", "kq")
        placed = (
            P(None, "lines", cells, None),
            P(cells, "lines"),
            P(),
            P(),
            P(("lines",) + cells),
            P("lines", None),
            P("lines", None),
            P(None, "lines", cells, None),
        )
        return jax.shard_map(
            on_device,
            mesh=split,
            in_specs=placed,
            out_specs=(P("lines", None), P(cells, "lines")),
            check_vma=False,
        )(*arrays)

    return run
```

```python
import math

import jax
import jax.numpy as jnp
from jax import lax
from jax.experimental import pallas as pl
from jax.experimental.pallas import tpu as pltpu
from jax.sharding import Mesh
from jax.sharding import PartitionSpec as P

ITERS = 2
INTERPRET = False


def halo(block, axis, dim, width):
    count = lax.axis_size(axis)
    edge_shape = list(block.shape)
    edge_shape[dim] = width
    if count == 1:
        zeros = jnp.zeros(edge_shape, block.dtype)
        return jnp.concatenate([zeros, block, zeros], axis=dim)
    forward = [(i, i + 1) for i in range(count - 1)]
    backward = [(target, source) for source, target in forward]
    low = lax.ppermute(
        lax.slice_in_dim(block, block.shape[dim] - width, None, axis=dim), axis, forward
    )
    high = lax.ppermute(lax.slice_in_dim(block, 0, width, axis=dim), axis, backward)
    return jnp.concatenate([low, block, high], axis=dim)


def next_column(field, axis):
    count = lax.axis_size(axis)
    if count == 1:
        edge = jnp.zeros_like(field[:, :, :1])
    else:
        edge = lax.ppermute(field[:, :, :1], axis, [(i + 1, i) for i in range(count - 1)])
    return jnp.concatenate([field[:, :, 1:], edge], axis=2)


def coefficients(sigma_wide):
    center = sigma_wide[1:-1]
    west_face = 0.5 * (center + sigma_wide[:-2])
    east_face = 0.5 * (center + sigma_wide[2:])
    below_sigma = jnp.concatenate([center[:, 1:], jnp.zeros_like(center[:, :1])], axis=1)
    lower_face = 0.5 * (center + below_sigma)
    above_sigma = jnp.concatenate([jnp.zeros_like(center[:, :1]), center[:, :-1]], axis=1)
    upper_face = 0.5 * (center + above_sigma)
    top_row = jnp.arange(center.shape[1]) == 0
    upper_face = jnp.where(top_row[None, :], 0.0, upper_face)
    return (west_face, east_face, lower_face, upper_face, center)


def stencil(field_wide, faces_set, mass_scale):
    west_face, east_face, lower_face, upper_face, center = faces_set
    middle = field_wide[..., 1:-1, :]
    below_cells = jnp.concatenate([middle[..., 1:], jnp.zeros_like(middle[..., :1])], axis=-1)
    above_cells = jnp.concatenate([jnp.zeros_like(middle[..., :1]), middle[..., :-1]], axis=-1)
    result = west_face * (middle - field_wide[..., :-2, :]) + east_face * (
        middle - field_wide[..., 2:, :]
    )
    result = result + lower_face * (middle - below_cells) + upper_face * (middle - above_cells)
    return result + mass_scale * center * middle


def pack_kernel(primary_ref, sigma_ref, send_ref):
    fields = primary_ref.shape[1]
    send_ref[:, 0:fields] = primary_ref[...]
    sigma = sigma_ref[...]
    for target in range(send_ref.shape[0]):
        send_ref[target, fields] = sigma


def pack(primary, sigma):
    groups, fields, rows, depth = primary.shape
    steps = 2 if groups % 2 == 0 else 1
    chunk = groups // steps
    return pl.pallas_call(
        pack_kernel,
        out_shape=jax.ShapeDtypeStruct((groups, fields + 1, rows, depth), jnp.float32),
        grid=(steps,),
        in_specs=[
            pl.BlockSpec((chunk, fields, rows, depth), lambda i: (i, 0, 0, 0)),
            pl.BlockSpec((rows, depth), lambda i: (0, 0)),
        ],
        out_specs=pl.BlockSpec((chunk, fields + 1, rows, depth), lambda i: (i, 0, 0, 0)),
        interpret=INTERPRET,
    )(primary, sigma)

def on_device(
    primary, conductivity, wavenumbers, quadrature, electrodes, far_pole, observed, prior_adjoint
):
    groups = lax.axis_size("kq")
    spread = lax.axis_size("cs")
    waves, sources, own_columns, depth = primary.shape
    per_group = waves // groups
    group = lax.axis_index("kq")
    block = lax.axis_index("cs")
    fields = per_group * sources

    def by_group(array):
        return array.reshape(groups, fields, own_columns, depth)

    send = pack(by_group(primary), conductivity)
    if groups > 1:
        send = lax.all_to_all(send, "kq", 0, 2, tiled=True)
    received = send[0]
    width = groups * own_columns
    primary = received[:fields].reshape(per_group, sources, width, depth)
    sigma = received[fields]
    chunk = fields * own_columns * depth
    packet_size = sources * width + electrodes.shape[0]
    prior_rows = jnp.concatenate(
        [prior_adjoint.reshape(groups, chunk), jnp.zeros((groups, packet_size), jnp.float32)], axis=1
    )

    columns = width * spread
    offset = block * width
    wide_sigma = halo(sigma, "cs", 0, 2)
    positions = offset - 2 + jnp.arange(width + 4)
    inside = (positions >= 0) & (positions < columns)
    contrast_wide = jnp.where(inside[:, None], wide_sigma - 1.0, 0.0)
    own_waves = lax.dynamic_slice_in_dim(wavenumbers, group * per_group, per_group)
    weights = lax.dynamic_slice_in_dim(quadrature, group * per_group, per_group)
    mass_scale = (own_waves * own_waves)[:, None, None, None]
    operator_faces = coefficients(wide_sigma[1:-1])

    def operate(state):
        return stencil(halo(state, "cs", 2, 1), operator_faces, mass_scale)

    def dots(left, right):
        total = jnp.sum(left * right, axis=(2, 3))
        if spread > 1:
            total = lax.psum(total, "cs")
        return total[:, :, None, None]

    def conjugate(source, start):
        if start is None:
            solution = jnp.zeros_like(source)
            residual = source
        else:
            solution = start
            residual = source - operate(start)
        direction = residual
        norm_now = dots(residual, residual)
        for iteration in range(ITERS):
            applied = operate(direction)
            step_size = norm_now / dots(direction, applied)
            solution = solution + step_size * direction
            if iteration + 1 < ITERS:
                residual = residual - step_size * applied
                norm_next = dots(residual, residual)
                direction = residual + (norm_next / norm_now) * direction
                norm_now = norm_next
        return solution

    source = -stencil(halo(primary, "cs", 2, 1), coefficients(contrast_wide[1:-1]), mass_scale)
    total_field = primary + conjugate(source, None)

    surface = total_field[:, :, :, 0]
    weighted = jnp.sum(weights[:, None, None] * surface, axis=0)
    packet = jnp.concatenate([weighted.reshape(-1), electrodes.astype(jnp.float32)])
    pole_hits = (far_pole[:, :, None] == jnp.arange(far_pole.shape[1])[None, None, :]).astype(jnp.float32)
    packet, pole_hits, held = lax.optimization_barrier((packet, pole_hits, 0.0 - observed))
    outgoing = jnp.broadcast_to(packet[None], (groups,) + packet.shape)
    outgoing = lax.dynamic_update_slice(prior_rows, outgoing, (0, chunk))
    if groups > 1:
        outgoing = lax.all_to_all(outgoing, "kq", 0, 0)
    prior_adjoint = outgoing[:, :chunk].reshape(groups, fields, own_columns, depth)
    prior_adjoint = prior_adjoint.transpose(1, 0, 2, 3).reshape(per_group, sources, width, depth)
    gathered = outgoing[:, chunk:]
    if spread > 1:
        gathered = lax.all_gather(gathered, "cs")
    gathered = gathered.reshape(spread * groups, -1)
    partial = gathered[:, : sources * width].reshape(spread, groups, sources, width)
    line_surface = jnp.sum(partial, axis=1).transpose(1, 0, 2).reshape(sources, columns)
    all_electrodes = gathered[:, sources * width :].reshape(-1).astype(jnp.int32)
    count = all_electrodes.shape[0]

    picks = (all_electrodes[:, None] == jnp.arange(columns)[None, :]).astype(jnp.float32)
    potentials = jnp.sum(line_surface[:, None, :] * picks[None], axis=2)
    far_potentials = jnp.sum(potentials[:, None, :] * pole_hits, axis=2)
    predicted = potentials - far_potentials
    misfit = predicted + held
    returned = jnp.sum(misfit[:, :, None] * pole_hits, axis=1)
    charge = misfit - returned
    own_picks = (
        all_electrodes[:, None] == offset + jnp.arange(width)[None, :]
    ).astype(jnp.float32)
    charge_cols = jnp.sum(charge[:, :, None] * own_picks[None], axis=1)
    surface_row = (jnp.arange(depth) == 0).astype(jnp.float32)
    adjoint_source = weights[:, None, None, None] * charge_cols[None, :, :, None] * surface_row
    adjoint = conjugate(adjoint_source, prior_adjoint)

    adjoint_next = next_column(adjoint, "cs")
    total_next = next_column(total_field, "cs")
    adjoint_down = jnp.concatenate([adjoint[..., 1:], jnp.zeros_like(adjoint[..., :1])], axis=-1)
    total_down = jnp.concatenate(
        [total_field[..., 1:], jnp.zeros_like(total_field[..., :1])], axis=-1
    )
    correlation = (adjoint_next - adjoint) * (total_next - total_field)
    correlation = correlation + (adjoint_down - adjoint) * (total_down - total_field)
    correlation = correlation + mass_scale * adjoint * total_field
    gradient = jnp.sum(correlation, axis=(0, 1))
    if groups > 1:
        gradient = gradient.reshape(groups, own_columns, depth)
        gradient = jnp.sum(lax.all_to_all(gradient, "kq", 0, 0, tiled=True), axis=0)
    return (predicted, gradient)


def solution(mesh):
    lines = mesh.shape["lines"]
    col = mesh.shape["col"]

    def run(*arrays):
        groups = math.gcd(col, arrays[0].shape[0])
        split = Mesh(mesh.devices.reshape(lines, col // groups, groups), ("lines", "cs", "kq"))
        cells = ("cs", "kq")
        placed = (
            P(None, "lines", cells, None),
            P(cells, "lines"),
            P(),
            P(),
            P(("lines",) + cells),
            P("lines", None),
            P("lines", None),
            P(None, "lines", cells, None),
        )
        return jax.shard_map(
            on_device,
            mesh=split,
            in_specs=placed,
            out_specs=(P("lines", None), P(cells, "lines")),
            check_vma=False,
        )(*arrays)

    return run
```

```python
import math

import jax
import jax.numpy as jnp
from jax import lax
from jax.experimental import pallas as pl
from jax.experimental.pallas import tpu as pltpu
from jax.sharding import Mesh
from jax.sharding import PartitionSpec as P

ITERS = 2
INTERPRET = False


def halo(block, axis, dim, width):
    count = lax.axis_size(axis)
    edge_shape = list(block.shape)
    edge_shape[dim] = width
    if count == 1:
        zeros = jnp.zeros(edge_shape, block.dtype)
        return jnp.concatenate([zeros, block, zeros], axis=dim)
    forward = [(i, i + 1) for i in range(count - 1)]
    backward = [(target, source) for source, target in forward]
    low = lax.ppermute(
        lax.slice_in_dim(block, block.shape[dim] - width, None, axis=dim), axis, forward
    )
    high = lax.ppermute(lax.slice_in_dim(block, 0, width, axis=dim), axis, backward)
    return jnp.concatenate([low, block, high], axis=dim)


def next_column(field, axis):
    count = lax.axis_size(axis)
    if count == 1:
        edge = jnp.zeros_like(field[:, :, :1])
    else:
        edge = lax.ppermute(field[:, :, :1], axis, [(i + 1, i) for i in range(count - 1)])
    return jnp.concatenate([field[:, :, 1:], edge], axis=2)


def coefficients(sigma_wide):
    center = sigma_wide[1:-1]
    west_face = 0.5 * (center + sigma_wide[:-2])
    east_face = 0.5 * (center + sigma_wide[2:])
    below_sigma = jnp.concatenate([center[:, 1:], jnp.zeros_like(center[:, :1])], axis=1)
    lower_face = 0.5 * (center + below_sigma)
    above_sigma = jnp.concatenate([jnp.zeros_like(center[:, :1]), center[:, :-1]], axis=1)
    upper_face = 0.5 * (center + above_sigma)
    top_row = jnp.arange(center.shape[1]) == 0
    upper_face = jnp.where(top_row[None, :], 0.0, upper_face)
    return (west_face, east_face, lower_face, upper_face, center)


def stencil(field_wide, faces_set, mass_scale):
    west_face, east_face, lower_face, upper_face, center = faces_set
    middle = field_wide[..., 1:-1, :]
    below_cells = jnp.concatenate([middle[..., 1:], jnp.zeros_like(middle[..., :1])], axis=-1)
    above_cells = jnp.concatenate([jnp.zeros_like(middle[..., :1]), middle[..., :-1]], axis=-1)
    result = west_face * (middle - field_wide[..., :-2, :]) + east_face * (
        middle - field_wide[..., 2:, :]
    )
    result = result + lower_face * (middle - below_cells) + upper_face * (middle - above_cells)
    return result + mass_scale * center * middle


def pack_kernel(primary_ref, sigma_ref, send_ref):
    fields = primary_ref.shape[1]
    send_ref[:, 0:fields] = primary_ref[...]
    sigma = sigma_ref[...]
    for target in range(send_ref.shape[0]):
        send_ref[target, fields] = sigma


def pack(primary, sigma):
    groups, fields, rows, depth = primary.shape
    steps = 2 if groups % 2 == 0 else 1
    chunk = groups // steps
    return pl.pallas_call(
        pack_kernel,
        out_shape=jax.ShapeDtypeStruct((groups, fields + 1, rows, depth), jnp.float32),
        grid=(steps,),
        in_specs=[
            pl.BlockSpec((chunk, fields, rows, depth), lambda i: (i, 0, 0, 0)),
            pl.BlockSpec((rows, depth), lambda i: (0, 0)),
        ],
        out_specs=pl.BlockSpec((chunk, fields + 1, rows, depth), lambda i: (i, 0, 0, 0)),
        interpret=INTERPRET,
    )(primary, sigma)

def on_device(
    primary, conductivity, wavenumbers, quadrature, electrodes, far_pole, observed, prior_adjoint
):
    groups = lax.axis_size("kq")
    spread = lax.axis_size("cs")
    waves, sources, own_columns, depth = primary.shape
    per_group = waves // groups
    group = lax.axis_index("kq")
    block = lax.axis_index("cs")
    fields = per_group * sources

    def by_group(array):
        return array.reshape(groups, fields, own_columns, depth)

    send = pack(by_group(primary), conductivity)
    if groups > 1:
        send = lax.all_to_all(send, "kq", 0, 2, tiled=True)
    received = send[0]
    width = groups * own_columns
    primary = received[:fields].reshape(per_group, sources, width, depth)
    sigma = received[fields]
    chunk = fields * own_columns * depth
    packet_size = sources * width + electrodes.shape[0]
    prior_rows = jnp.concatenate(
        [prior_adjoint.reshape(groups, chunk), jnp.zeros((groups, packet_size), jnp.float32)], axis=1
    )

    columns = width * spread
    offset = block * width
    wide_sigma = halo(sigma, "cs", 0, 2)
    positions = offset - 2 + jnp.arange(width + 4)
    inside = (positions >= 0) & (positions < columns)
    contrast_wide = jnp.where(inside[:, None], wide_sigma - 1.0, 0.0)
    own_waves = lax.dynamic_slice_in_dim(wavenumbers, group * per_group, per_group)
    weights = lax.dynamic_slice_in_dim(quadrature, group * per_group, per_group)
    mass_scale = (own_waves * own_waves)[:, None, None, None]
    weight_rows = jnp.broadcast_to(weights[:, None, None], (per_group, sources, width))
    prior_rows, weight_rows = lax.optimization_barrier((prior_rows, weight_rows))
    operator_faces = coefficients(wide_sigma[1:-1])

    def operate(state):
        return stencil(halo(state, "cs", 2, 1), operator_faces, mass_scale)

    def dots(left, right):
        total = jnp.sum(left * right, axis=(2, 3))
        if spread > 1:
            total = lax.psum(total, "cs")
        return total[:, :, None, None]

    def conjugate(source, start):
        if start is None:
            solution = jnp.zeros_like(source)
            residual = source
        else:
            solution = start
            residual = source - operate(start)
        direction = residual
        norm_now = dots(residual, residual)
        for iteration in range(ITERS):
            applied = operate(direction)
            step_size = norm_now / dots(direction, applied)
            solution = solution + step_size * direction
            if iteration + 1 < ITERS:
                residual = residual - step_size * applied
                norm_next = dots(residual, residual)
                direction = residual + (norm_next / norm_now) * direction
                norm_now = norm_next
        return solution

    source = -stencil(halo(primary, "cs", 2, 1), coefficients(contrast_wide[1:-1]), mass_scale)
    total_field = primary + conjugate(source, None)

    surface = total_field[:, :, :, 0]
    weighted = jnp.sum(weight_rows * surface, axis=0)
    packet = jnp.concatenate([weighted.reshape(-1), electrodes.astype(jnp.float32)])
    pole_hits = (far_pole[:, :, None] == jnp.arange(far_pole.shape[1])[None, None, :]).astype(jnp.float32)
    packet, pole_hits, held = lax.optimization_barrier((packet, pole_hits, 0.0 - observed))
    outgoing = jnp.broadcast_to(packet[None], (groups,) + packet.shape)
    outgoing = lax.dynamic_update_slice(prior_rows, outgoing, (0, chunk))
    if groups > 1:
        outgoing = lax.all_to_all(outgoing, "kq", 0, 0)
    prior_adjoint = outgoing[:, :chunk].reshape(groups, fields, own_columns, depth)
    prior_adjoint = prior_adjoint.transpose(1, 0, 2, 3).reshape(per_group, sources, width, depth)
    gathered = outgoing[:, chunk:]
    if spread > 1:
        gathered = lax.all_gather(gathered, "cs")
    gathered = gathered.reshape(spread * groups, -1)
    partial = gathered[:, : sources * width].reshape(spread, groups, sources, width)
    line_surface = jnp.sum(partial, axis=1).transpose(1, 0, 2).reshape(sources, columns)
    all_electrodes = gathered[:, sources * width :].reshape(-1).astype(jnp.int32)
    count = all_electrodes.shape[0]

    picks = (all_electrodes[:, None] == jnp.arange(columns)[None, :]).astype(jnp.float32)
    potentials = jnp.sum(line_surface[:, None, :] * picks[None], axis=2)
    far_potentials = jnp.sum(potentials[:, None, :] * pole_hits, axis=2)
    predicted = potentials - far_potentials
    misfit = predicted + held
    returned = jnp.sum(misfit[:, :, None] * pole_hits, axis=1)
    charge = misfit - returned
    own_picks = (
        all_electrodes[:, None] == offset + jnp.arange(width)[None, :]
    ).astype(jnp.float32)
    charge_cols = jnp.sum(charge[:, :, None] * own_picks[None], axis=1)
    surface_row = (jnp.arange(depth) == 0).astype(jnp.float32)
    adjoint_source = (weight_rows * charge_cols[None])[..., None] * surface_row
    adjoint = conjugate(adjoint_source, prior_adjoint)

    adjoint_next = next_column(adjoint, "cs")
    total_next = next_column(total_field, "cs")
    adjoint_down = jnp.concatenate([adjoint[..., 1:], jnp.zeros_like(adjoint[..., :1])], axis=-1)
    total_down = jnp.concatenate(
        [total_field[..., 1:], jnp.zeros_like(total_field[..., :1])], axis=-1
    )
    correlation = (adjoint_next - adjoint) * (total_next - total_field)
    correlation = correlation + (adjoint_down - adjoint) * (total_down - total_field)
    correlation = correlation + mass_scale * adjoint * total_field
    gradient = jnp.sum(correlation, axis=(0, 1))
    if groups > 1:
        gradient = gradient.reshape(groups, own_columns, depth)
        gradient = jnp.sum(lax.all_to_all(gradient, "kq", 0, 0, tiled=True), axis=0)
    return (predicted, gradient)


def solution(mesh):
    lines = mesh.shape["lines"]
    col = mesh.shape["col"]

    def run(*arrays):
        groups = math.gcd(col, arrays[0].shape[0])
        split = Mesh(mesh.devices.reshape(lines, col // groups, groups), ("lines", "cs", "kq"))
        cells = ("cs", "kq")
        placed = (
            P(None, "lines", cells, None),
            P(cells, "lines"),
            P(),
            P(),
            P(("lines",) + cells),
            P("lines", None),
            P("lines", None),
            P(None, "lines", cells, None),
        )
        return jax.shard_map(
            on_device,
            mesh=split,
            in_specs=placed,
            out_specs=(P("lines", None), P(cells, "lines")),
            check_vma=False,
        )(*arrays)

    return run
```
